256 devices in a mesh: rep: 4 (over x), exp: 64 (over y, z, core).
Axes of the slice: x: 4, y: 4, z: 8, core: 2. Of those that a mesh axis runs over, the one named last changes fastest.
Arguments:
- tokens: bfloat16 [32768, 2048], P(('rep', 'exp')), may hold values from -6 to 6
- grad_out: bfloat16 [32768, 2048], P(('rep', 'exp')), may hold values from -6 to 6
- routes: int32 [32768, 2], P(('rep', 'exp')), may hold values from 0 to 63, all different within a row; in each aligned block of 128 rows (0 to 127, 128 to 255, ...) at most 8 rows name the same one
- gates: float32 [32768, 2], P(('rep', 'exp')), may hold values from 0.1 to 1
- w_gate: bfloat16 [64, 2048, 768], P('exp', 'rep'), may hold values from -0.125 to 0.125
- w_up: bfloat16 [64, 2048, 768], P('exp', 'rep'), may hold values from -0.125 to 0.125
- w_down: bfloat16 [64, 2048, 768], P('exp', 'rep'), may hold values from -0.125 to 0.125
Outputs:
- grad_gate: float32 [64, 2048, 768], P('exp', 'rep')
- grad_up: float32 [64, 2048, 768], P('exp', 'rep')
- grad_down: float32 [64, 2048, 768], P('exp', 'rep')
- grad_in: bfloat16 [32768, 2048], P(('rep', 'exp'))
The draws below stay inside these ranges and needn't reach their ends.
Inputs may be any that keep to these rules, and one draw needn't show every extreme that they name: `routes`: each row names 2 different experts. Among the 128 rows of one device no expert is named more than 8 times, and in every draw some device names some expert exactly 8 times; every expert is named somewhere.
All inputs are finite; a program needn't handle non-finite values.
Results may differ from the reference program's by a relative error of at most 0.0065.
Values may be sent and summed in bfloat16 or wider, within the bound.
No kernel may reach another device: no remote copies, remote signals or barrier semaphores. Data moves between devices by JAX's collectives and lax.ppermute only.
A program may use at most 128 MiB of HBM per device.

```python
import math
import jax
import jax.numpy as jnp
import numpy as np
from jax import lax

D = 2048
FF = 768
TOPK = 2
TOK_DEV = 128
EXPERTS = 64
CAP = 8
TOKENS = 32768


def levels(key, shape, split, least, largest):
    gain = 1.0
    for dim, parts in split:
        heights = jax.random.uniform(jax.random.fold_in(jax.random.fold_in(key, 6), dim), (parts,), jnp.float32, least / len(split), largest / len(split))
        gain = gain * jnp.repeat(jnp.exp(heights), shape[dim] // parts).reshape((-1,) + (1,) * (len(shape) - 1 - dim))
    return gain


def routed_block(own_key, own, number, rows, number_of, top, reach, skew):
    sequence = jax.random.permutation(own_key, number_of)
    packed, ordinary = load_shares(number_of, rows * top, reach, skew, True), load_shares(number_of, rows * top, reach, skew, False)
    places = jnp.arange(number_of)

    def named(lengths, rotation):
        used = int((lengths > 0).sum())
        fixed = max(1, used // 4)
        passed = fixed + (places - fixed + rotation * (used - fixed)) % max(1, number_of - fixed)
        return jnp.zeros((number_of,), jnp.int32).at[sequence[jnp.where(places < fixed, places, passed)]].set(jnp.asarray(lengths, jnp.int32))

    lengths = jnp.where(number % 4 == 0, named(packed, number // 4), named(ordinary, number - number // 4 - 1))
    mixed = jax.random.permutation(jax.random.fold_in(own, 3), number_of)
    donor, taker = mixed[0:number_of // 2 * 2:2], mixed[1:number_of // 2 * 2:2]
    room = jnp.minimum(lengths[donor] - 1, reach - lengths[taker]) // 2
    room = jnp.where((donor == sequence[0]) | (taker == sequence[0]) | (lengths[taker] == 0), 0, jnp.maximum(room, 0))
    passed = jax.random.randint(jax.random.fold_in(own, 4), (number_of // 2,), 0, 1 << 20) % (room + 1)
    lengths = lengths.at[donor].add(-passed).at[taker].add(passed)
    labels = jnp.searchsorted(jnp.cumsum(lengths), jnp.arange(rows * top), side="right").astype(jnp.int32)
    table = labels.reshape(top, rows).T
    table = table[jax.random.permutation(jax.random.fold_in(own, 1), rows)]
    rotation = jax.random.randint(jax.random.fold_in(own, 2), (rows, 1), 0, top)
    return jnp.take_along_axis(table, (jnp.arange(top)[None, :] + rotation) % top, axis=1)


def load_shares(count, total, most, lean, full):
    portions = [(1 << 20) // math.isqrt(standing ** lean) + 1 for standing in range(1, count + 1)]
    largest = most if full else min(most, max(-(-total // count), total * portions[0] // sum(portions)))
    least = 1 if total - largest >= count - 1 else 0
    given, rest = [largest] + [least] * (count - 1), total - largest - least * (count - 1)
    while rest > 0:
        free = [i for i in range(1, count) if given[i] < largest] or [i for i in range(1, count) if given[i] < most]
        mass, remaining = sum([portions[i] for i in free]), rest
        for i in free:
            extra = min(most - given[i], max(1, remaining * portions[i] // mass), rest)
            given[i] = given[i] + extra
            rest = rest - extra
    return np.array(given)


def scatter_about(key, dims, spread, bound, split=(), held_as=jnp.bfloat16):
    drawn = spread * jax.random.normal(key, dims, jnp.float32)
    if split:
        drawn = drawn * levels(key, dims, split, -0.22, 0.18)
    return jnp.clip(drawn, -bound, bound).astype(held_as)


def setup_inputs(seed: int = 0) -> dict:
    keys = jax.random.split(jax.random.key(seed), 8)
    tokens = scatter_about(keys[0], (TOKENS, D), 1.0, 6.0, ((0, 256),))
    grad_out = scatter_about(keys[1], (TOKENS, D), 1.0, 6.0, ((0, 256),))
    routes_keys = jax.random.split(jax.random.fold_in(keys[2], 1), TOKENS // TOK_DEV)
    routes_turns = jax.random.permutation(jax.random.fold_in(keys[2], 3), TOKENS // TOK_DEV)
    routes = jax.vmap(lambda own, number: routed_block(jax.random.fold_in(keys[2], 2), own, number, TOK_DEV, EXPERTS, TOPK, CAP, 2))(routes_keys, routes_turns).reshape((TOKENS, TOPK))
    gates = jnp.clip(0.1 + 0.9 * jax.random.uniform(keys[3], (TOKENS, TOPK), jnp.float32) ** levels(keys[3], (TOKENS, TOPK), ((0, 256),), -0.2, 0.2), 0.1, 1.0)
    w_gate = scatter_about(keys[4], (EXPERTS, D, FF), D ** -0.5, 0.125, ((0, 64), (1, 4)))
    w_up = scatter_about(keys[5], (EXPERTS, D, FF), D ** -0.5, 0.125, ((0, 64), (1, 4)))
    w_down = scatter_about(keys[6], (EXPERTS, D, FF), D ** -0.5, 0.125, ((0, 64), (1, 4)))
    return {"tokens": tokens, "grad_out": grad_out, "routes": routes, "gates": gates, "w_gate": w_gate, "w_up": w_up, "w_down": w_down}


block_rows = 512


def contract_rows(left, right):
    return lax.dot_general(left, right, (((0,), (0,)), ((), ())), preferred_element_type=jnp.float32)


def against_cols(left, right):
    return lax.dot_general(left, right, (((1,), (1,)), ((), ())), preferred_element_type=jnp.float32)


def reference(tokens, grad_out, routes, gates, w_gate, w_up, w_down):
    tok_total = tokens.shape[0]
    route_total = tok_total * TOPK
    flat_routes = routes.reshape(-1).astype(jnp.int32)
    order = jnp.argsort(flat_routes, stable=True).astype(jnp.int32)
    expert_ids = jnp.arange(EXPERTS, dtype=jnp.int32)
    counts = jnp.sum((flat_routes[:, None] == expert_ids[None, :]).astype(jnp.int32), axis=0)
    starts = (jnp.cumsum(counts) - counts).astype(jnp.int32)
    order_pad = jnp.concatenate([order, jnp.zeros((block_rows,), jnp.int32)])
    scaled_all = (gates[:, :, None].astype(jnp.float32) * grad_out[:, None, :].astype(jnp.float32)).astype(jnp.bfloat16)
    scaled_all = scaled_all.reshape(route_total, D)
    lanes = jnp.arange(block_rows, dtype=jnp.int32)

    def expert_step(accum, expert):
        gate_mat = w_gate[expert]
        up_mat = w_up[expert]
        down_mat = w_down[expert]
        block_count = (counts[expert] + block_rows - 1) // block_rows

        def block_step(block_idx, state):
            dx_acc, acc_gate, acc_up, acc_down = state
            offset = (starts[expert] + block_idx * block_rows).astype(jnp.int32)
            picked = lax.dynamic_slice(order_pad, (offset,), (block_rows,))
            live_mask = (block_idx * block_rows + lanes) < counts[expert]
            tok_ids = picked // TOPK
            x_rows = jnp.where(live_mask[:, None], tokens[tok_ids], jnp.zeros((), jnp.bfloat16))
            g_rows = jnp.where(live_mask[:, None], scaled_all[picked], jnp.zeros((), jnp.bfloat16))
            pre_gate = jnp.dot(x_rows, gate_mat, preferred_element_type=jnp.float32)
            pre_up = jnp.dot(x_rows, up_mat, preferred_element_type=jnp.float32)
            sig_gate = jax.nn.sigmoid(pre_gate)
            silu_gate = pre_gate * sig_gate
            hidden = (silu_gate * pre_up).astype(jnp.bfloat16)
            hid_grad = jnp.dot(g_rows, down_mat, preferred_element_type=jnp.float32)
            d_gate = (hid_grad * pre_up * sig_gate * (1.0 + pre_gate * (1.0 - sig_gate))).astype(jnp.bfloat16)
            d_up = (hid_grad * silu_gate).astype(jnp.bfloat16)
            acc_gate = acc_gate + contract_rows(x_rows, d_gate)
            acc_up = acc_up + contract_rows(x_rows, d_up)
            acc_down = acc_down + contract_rows(g_rows, hidden)
            row_grad = (against_cols(d_gate, gate_mat) + against_cols(d_up, up_mat)).astype(jnp.bfloat16)
            contrib = jnp.where(live_mask[:, None], row_grad.astype(jnp.float32), jnp.zeros((), jnp.float32))
            dx_acc = dx_acc.at[tok_ids].add(contrib)
            return dx_acc, acc_gate, acc_up, acc_down

        zero_grad = jnp.zeros((D, FF), jnp.float32)
        result = lax.fori_loop(0, block_count, block_step, (accum, zero_grad, zero_grad, zero_grad))
        return result[0], (result[1], result[2], result[3])

    dx_total, grads = lax.scan(expert_step, jnp.zeros((tok_total, D), jnp.float32), expert_ids)
    return grads[0], grads[1], grads[2], dx_total.astype(jnp.bfloat16)
```

```python
import jax
import jax.numpy as jnp
from jax import lax
from jax.sharding import PartitionSpec as P


def contract_rows(left, right):
    return lax.dot_general(
        left, right, (((0,), (0,)), ((), ())), preferred_element_type=jnp.float32
    )


def against_cols(left, right):
    return lax.dot_general(
        left, right, (((1,), (1,)), ((), ())), preferred_element_type=jnp.float32
    )


def per_device(tokens, grad_out, routes, gates, w_gate, w_up, w_down):
    tok_count, model_width = tokens.shape
    route_count = routes.shape[1]
    expert_count = lax.axis_size("exp")
    slot_cap = max(2, 2 * tok_count * route_count // expert_count)
    route_total = tok_count * route_count
    slot_total = expert_count * slot_cap
    flat_routes = routes.reshape(-1)
    onehot = (flat_routes[:, None] == jnp.arange(expert_count, dtype=jnp.int32)[None, :]).astype(
        jnp.int32
    )
    slot_rank = jnp.sum((jnp.cumsum(onehot, axis=0) - 1) * onehot, axis=1)
    slot_index = flat_routes * slot_cap + slot_rank
    source = (
        jnp.full((slot_total,), route_total, jnp.int32)
        .at[slot_index]
        .set(jnp.arange(route_total, dtype=jnp.int32))
    )
    scaled = (gates[:, :, None] * grad_out[:, None, :].astype(jnp.float32)).astype(jnp.bfloat16)
    scaled = scaled.reshape(route_total, model_width)
    zero_row = jnp.zeros((1, model_width), jnp.bfloat16)
    tok_pad = jnp.concatenate([tokens, zero_row], axis=0)
    scaled_pad = jnp.concatenate([scaled, zero_row], axis=0)
    tok_source = jnp.where(source < route_total, source // route_count, tok_count)
    x_send = tok_pad[tok_source]
    g_send = scaled_pad[source]
    both_recv = lax.all_to_all(
        jnp.concatenate([x_send, g_send], axis=1), "exp", split_axis=0, concat_axis=0, tiled=True
    )
    x_recv = both_recv[:, :model_width]
    g_recv = both_recv[:, model_width:]
    full_all = lax.all_gather(
        jnp.stack([w_gate[0], w_up[0], w_down[0]], axis=0), "rep", axis=1, tiled=True
    )
    full_gate, full_up, full_down = full_all[0], full_all[1], full_all[2]
    pre_gate = jnp.dot(x_recv, full_gate, preferred_element_type=jnp.float32)
    pre_up = jnp.dot(x_recv, full_up, preferred_element_type=jnp.float32)
    hid_grad = jnp.dot(g_recv, full_down, preferred_element_type=jnp.float32)
    sig_gate = jax.nn.sigmoid(pre_gate)
    silu_gate = pre_gate * sig_gate
    hidden = (silu_gate * pre_up).astype(jnp.bfloat16)
    d_gate = (hid_grad * pre_up * sig_gate * (1.0 + pre_gate * (1.0 - sig_gate))).astype(
        jnp.bfloat16
    )
    d_up = (hid_grad * silu_gate).astype(jnp.bfloat16)
    row_grad = (against_cols(d_gate, full_gate) + against_cols(d_up, full_up)).astype(jnp.bfloat16)
    returned = lax.all_to_all(row_grad, "exp", split_axis=0, concat_axis=0, tiled=True)
    picked = returned[slot_index].reshape(tok_count, route_count, model_width)
    grad_in = jnp.sum(picked.astype(jnp.float32), axis=1).astype(jnp.bfloat16)
    summed = lax.psum_scatter(
        jnp.stack(
            [
                contract_rows(x_recv, d_gate),
                contract_rows(x_recv, d_up),
                contract_rows(g_recv, hidden),
            ],
            axis=1,
        ).astype(jnp.bfloat16),
        "rep",
        scatter_dimension=0,
        tiled=True,
    )
    summed = summed.astype(jnp.float32)
    grad_gate = summed[:, 0, :]
    grad_up = summed[:, 1, :]
    grad_down = summed[:, 2, :]
    return (grad_gate[None], grad_up[None], grad_down[None], grad_in)


def solution(mesh):
    placed = (
        P(("rep", "exp"), None),
        P(("rep", "exp"), None),
        P(("rep", "exp"), None),
        P(("rep", "exp"), None),
        P("exp", "rep", None),
        P("exp", "rep", None),
        P("exp", "rep", None),
    )
    return jax.shard_map(
        per_device,
        mesh=mesh,
        in_specs=placed,
        out_specs=(
            P("exp", "rep", None),
            P("exp", "rep", None),
            P("exp", "rep", None),
            P(("rep", "exp"), None),
        ),
        check_vma=False,
    )
```

```python
import jax
import jax.numpy as jnp
from jax import lax
from jax.sharding import PartitionSpec as P


def contract_rows(left, right):
    return lax.dot_general(
        left, right, (((0,), (0,)), ((), ())), preferred_element_type=jnp.float32
    )


def against_cols(left, right):
    return lax.dot_general(
        left, right, (((1,), (1,)), ((), ())), preferred_element_type=jnp.float32
    )


def per_device(tokens, grad_out, routes, gates, w_gate, w_up, w_down):
    tok_count, model_width = tokens.shape
    route_count = routes.shape[1]
    expert_count = lax.axis_size("exp")
    slot_cap = max(2, 2 * tok_count * route_count // expert_count)
    route_total = tok_count * route_count
    slot_total = expert_count * slot_cap
    flat_routes = routes.reshape(-1)
    onehot = (flat_routes[:, None] == jnp.arange(expert_count, dtype=jnp.int32)[None, :]).astype(
        jnp.int32
    )
    slot_rank = jnp.sum((jnp.cumsum(onehot, axis=0) - 1) * onehot, axis=1)
    slot_index = flat_routes * slot_cap + slot_rank
    source = (
        jnp.full((slot_total,), route_total, jnp.int32)
        .at[slot_index]
        .set(jnp.arange(route_total, dtype=jnp.int32))
    )
    scaled = (gates[:, :, None] * grad_out[:, None, :].astype(jnp.float32)).astype(jnp.bfloat16)
    table = jnp.concatenate(
        [
            jnp.broadcast_to(tokens[:, None, :], (tok_count, route_count, model_width)),
            scaled,
        ],
        axis=2,
    ).reshape(route_total, 2 * model_width)
    table = jnp.concatenate([table, jnp.zeros((1, 2 * model_width), jnp.bfloat16)], axis=0)
    both_recv = lax.all_to_all(table[source], "exp", split_axis=0, concat_axis=0, tiled=True)
    x_recv = both_recv[:, :model_width]
    g_recv = both_recv[:, model_width:]
    full_all = lax.all_gather(
        jnp.stack([w_gate[0], w_up[0], w_down[0]], axis=0), "rep", axis=1, tiled=True
    )
    full_gate, full_up, full_down = full_all[0], full_all[1], full_all[2]
    pre_gate = jnp.dot(x_recv, full_gate, preferred_element_type=jnp.float32)
    pre_up = jnp.dot(x_recv, full_up, preferred_element_type=jnp.float32)
    hid_grad = jnp.dot(g_recv, full_down, preferred_element_type=jnp.float32)
    sig_gate = jax.nn.sigmoid(pre_gate)
    silu_gate = pre_gate * sig_gate
    hidden = (silu_gate * pre_up).astype(jnp.bfloat16)
    d_gate = (hid_grad * pre_up * sig_gate * (1.0 + pre_gate * (1.0 - sig_gate))).astype(
        jnp.bfloat16
    )
    d_up = (hid_grad * silu_gate).astype(jnp.bfloat16)
    row_grad = (against_cols(d_gate, full_gate) + against_cols(d_up, full_up)).astype(jnp.bfloat16)
    returned = lax.all_to_all(row_grad, "exp", split_axis=0, concat_axis=0, tiled=True)
    picked = returned[slot_index].reshape(tok_count, route_count, model_width)
    grad_in = jnp.sum(picked.astype(jnp.float32), axis=1).astype(jnp.bfloat16)
    summed = lax.psum_scatter(
        jnp.stack(
            [
                contract_rows(x_recv, d_gate),
                contract_rows(x_recv, d_up),
                contract_rows(g_recv, hidden),
            ],
            axis=0,
        ).astype(jnp.bfloat16),
        "rep",
        scatter_dimension=1,
        tiled=True,
    )
    summed = summed.astype(jnp.float32)
    grad_gate = summed[0]
    grad_up = summed[1]
    grad_down = summed[2]
    return (grad_gate[None], grad_up[None], grad_down[None], grad_in)


def solution(mesh):
    placed = (
        P(("rep", "exp"), None),
        P(("rep", "exp"), None),
        P(("rep", "exp"), None),
        P(("rep", "exp"), None),
        P("exp", "rep", None),
        P("exp", "rep", None),
        P("exp", "rep", None),
    )
    return jax.shard_map(
        per_device,
        mesh=mesh,
        in_specs=placed,
        out_specs=(
            P("exp", "rep", None),
            P("exp", "rep", None),
            P("exp", "rep", None),
            P(("rep", "exp"), None),
        ),
        check_vma=False,
    )
```

```python
import jax
import jax.numpy as jnp
from jax import lax
from jax.sharding import PartitionSpec as P


def contract_rows(left, right):
    return lax.dot_general(
        left, right, (((0,), (0,)), ((), ())), preferred_element_type=jnp.float32
    )


def against_cols(left, right):
    return lax.dot_general(
        left, right, (((1,), (1,)), ((), ())), preferred_element_type=jnp.float32
    )


def per_device(tokens, grad_out, routes, gates, w_gate, w_up, w_down):
    tok_count, model_width = tokens.shape
    route_count = routes.shape[1]
    expert_count = lax.axis_size("exp")
    slot_cap = max(2, 2 * tok_count * route_count // expert_count)
    route_total = tok_count * route_count
    slot_total = expert_count * slot_cap
    flat_routes = routes.reshape(-1)
    onehot = (flat_routes[:, None] == jnp.arange(expert_count, dtype=jnp.int32)[None, :]).astype(
        jnp.int32
    )
    slot_rank = jnp.sum((jnp.cumsum(onehot, axis=0) - 1) * onehot, axis=1)
    slot_index = flat_routes * slot_cap + slot_rank
    source = (
        jnp.full((slot_total,), route_total, jnp.int32)
        .at[slot_index]
        .set(jnp.arange(route_total, dtype=jnp.int32))
    )
    tok_source = jnp.where(source < route_total, source // route_count, tok_count)
    pair_rows = jnp.concatenate(
        [jnp.concatenate([tokens, grad_out], axis=1), jnp.zeros((1, 2 * model_width), jnp.bfloat16)],
        axis=0,
    )[tok_source]
    gate_of = jnp.concatenate([gates.reshape(-1), jnp.zeros((1,), gates.dtype)])[source]
    row_scale = jnp.where(
        jnp.arange(2 * model_width)[None, :] < model_width, jnp.ones((), gates.dtype), gate_of[:, None]
    )
    send = (pair_rows.astype(jnp.float32) * row_scale).astype(jnp.bfloat16)
    both_recv = lax.all_to_all(
        send.reshape(slot_total, 2 * model_width), "exp", split_axis=0, concat_axis=0, tiled=True
    )
    x_recv = both_recv[:, :model_width]
    g_recv = both_recv[:, model_width:]
    full_all = lax.all_gather(
        jnp.stack([w_gate[0], w_up[0], w_down[0]], axis=0), "rep", axis=1, tiled=True
    )
    full_gate, full_up, full_down = full_all[0], full_all[1], full_all[2]
    pre_gate = jnp.dot(x_recv, full_gate, preferred_element_type=jnp.float32)
    pre_up = jnp.dot(x_recv, full_up, preferred_element_type=jnp.float32)
    hid_grad = jnp.dot(g_recv, full_down, preferred_element_type=jnp.float32)
    sig_gate = jax.nn.sigmoid(pre_gate)
    silu_gate = pre_gate * sig_gate
    hidden = (silu_gate * pre_up).astype(jnp.bfloat16)
    d_gate = (hid_grad * pre_up * sig_gate * (1.0 + pre_gate * (1.0 - sig_gate))).astype(
        jnp.bfloat16
    )
    d_up = (hid_grad * silu_gate).astype(jnp.bfloat16)
    row_grad = (against_cols(d_gate, full_gate) + against_cols(d_up, full_up)).astype(jnp.bfloat16)
    returned = lax.all_to_all(row_grad, "exp", split_axis=0, concat_axis=0, tiled=True)
    picked = returned[slot_index].reshape(tok_count, route_count, model_width)
    grad_in = jnp.sum(picked.astype(jnp.float32), axis=1).astype(jnp.bfloat16)
    summed = lax.psum_scatter(
        jnp.stack(
            [
                contract_rows(x_recv, d_gate),
                contract_rows(x_recv, d_up),
                contract_rows(g_recv, hidden),
            ],
            axis=0,
        ).astype(jnp.bfloat16),
        "rep",
        scatter_dimension=1,
        tiled=True,
    )
    summed = summed.astype(jnp.float32)
    grad_gate = summed[0]
    grad_up = summed[1]
    grad_down = summed[2]
    return (grad_gate[None], grad_up[None], grad_down[None], grad_in)


def solution(mesh):
    placed = (
        P(("rep", "exp"), None),
        P(("rep", "exp"), None),
        P(("rep", "exp"), None),
        P(("rep", "exp"), None),
        P("exp", "rep", None),
        P("exp", "rep", None),
        P("exp", "rep", None),
    )
    return jax.shard_map(
        per_device,
        mesh=mesh,
        in_specs=placed,
        out_specs=(
            P("exp", "rep", None),
            P("exp", "rep", None),
            P("exp", "rep", None),
            P(("rep", "exp"), None),
        ),
        check_vma=False,
    )
```

```python
import jax
import jax.numpy as jnp
from jax import lax
from jax.sharding import PartitionSpec as P


def contract_rows(left, right):
    return lax.dot_general(
        left, right, (((0,), (0,)), ((), ())), preferred_element_type=jnp.float32
    )


def against_cols(left, right):
    return lax.dot_general(
        left, right, (((1,), (1,)), ((), ())), preferred_element_type=jnp.float32
    )


def per_device(tokens, grad_out, routes, gates, w_gate, w_up, w_down):
    tok_count, model_width = tokens.shape
    route_count = routes.shape[1]
    expert_count = lax.axis_size("exp")
    slot_cap = max(2, 2 * tok_count * route_count // expert_count)
    route_total = tok_count * route_count
    slot_total = expert_count * slot_cap
    flat_routes = routes.reshape(-1)
    onehot = (flat_routes[:, None] == jnp.arange(expert_count, dtype=jnp.int32)[None, :]).astype(
        jnp.int32
    )
    slot_rank = jnp.sum((jnp.cumsum(onehot, axis=0) - 1) * onehot, axis=1)
    slot_index = flat_routes * slot_cap + slot_rank
    source = (
        jnp.full((slot_total,), route_total, jnp.int32)
        .at[slot_index]
        .set(jnp.arange(route_total, dtype=jnp.int32))
    )
    table = jnp.concatenate(
        [
            jnp.concatenate(
                [
                    tokens,
                    (gates[:, k : k + 1] * grad_out.astype(jnp.float32)).astype(jnp.bfloat16),
                ],
                axis=1,
            )
            for k in range(route_count)
        ]
        + [jnp.zeros((1, 2 * model_width), jnp.bfloat16)],
        axis=0,
    )
    by_choice = jnp.where(
        source < route_total,
        (source % route_count) * tok_count + source // route_count,
        route_total,
    )
    both_recv = lax.all_to_all(table[by_choice], "exp", split_axis=0, concat_axis=0, tiled=True)
    x_recv = both_recv[:, :model_width]
    g_recv = both_recv[:, model_width:]
    full_all = lax.all_gather(
        jnp.stack([w_gate[0], w_up[0], w_down[0]], axis=0), "rep", axis=1, tiled=True
    )
    full_gate, full_up, full_down = full_all[0], full_all[1], full_all[2]
    pre_gate = jnp.dot(x_recv, full_gate, preferred_element_type=jnp.float32)
    pre_up = jnp.dot(x_recv, full_up, preferred_element_type=jnp.float32)
    hid_grad = jnp.dot(g_recv, full_down, preferred_element_type=jnp.float32)
    sig_gate = jax.nn.sigmoid(pre_gate)
    silu_gate = pre_gate * sig_gate
    hidden = (silu_gate * pre_up).astype(jnp.bfloat16)
    d_gate = (hid_grad * pre_up * sig_gate * (1.0 + pre_gate * (1.0 - sig_gate))).astype(
        jnp.bfloat16
    )
    d_up = (hid_grad * silu_gate).astype(jnp.bfloat16)
    row_grad = (against_cols(d_gate, full_gate) + against_cols(d_up, full_up)).astype(jnp.bfloat16)
    returned = lax.all_to_all(row_grad, "exp", split_axis=0, concat_axis=0, tiled=True)
    picked = returned[slot_index].reshape(tok_count, route_count, model_width)
    grad_in = jnp.sum(picked.astype(jnp.float32), axis=1).astype(jnp.bfloat16)
    summed = lax.psum_scatter(
        jnp.stack(
            [
                contract_rows(x_recv, d_gate),
                contract_rows(x_recv, d_up),
                contract_rows(g_recv, hidden),
            ],
            axis=0,
        ).astype(jnp.bfloat16),
        "rep",
        scatter_dimension=1,
        tiled=True,
    )
    summed = summed.astype(jnp.float32)
    grad_gate = summed[0]
    grad_up = summed[1]
    grad_down = summed[2]
    return (grad_gate[None], grad_up[None], grad_down[None], grad_in)


def solution(mesh):
    placed = (
        P(("rep", "exp"), None),
        P(("rep", "exp"), None),
        P(("rep", "exp"), None),
        P(("rep", "exp"), None),
        P("exp", "rep", None),
        P("exp", "rep", None),
        P("exp", "rep", None),
    )
    return jax.shard_map(
        per_device,
        mesh=mesh,
        in_specs=placed,
        out_specs=(
            P("exp", "rep", None),
            P("exp", "rep", None),
            P("exp", "rep", None),
            P(("rep", "exp"), None),
        ),
        check_vma=False,
    )
```

```python
import jax
import jax.numpy as jnp
from jax import lax
from jax.sharding import PartitionSpec as P


def contract_rows(left, right):
    return lax.dot_general(
        left, right, (((0,), (0,)), ((), ())), preferred_element_type=jnp.float32
    )


def against_cols(left, right):
    return lax.dot_general(
        left, right, (((1,), (1,)), ((), ())), preferred_element_type=jnp.float32
    )


def per_device(tokens, grad_out, routes, gates, w_gate, w_up, w_down):
    tok_count, model_width = tokens.shape
    route_count = routes.shape[1]
    expert_count = lax.axis_size("exp")
    slot_cap = max(2, 2 * tok_count * route_count // expert_count)
    route_total = tok_count * route_count
    slot_total = expert_count * slot_cap
    flat_routes = routes.reshape(-1)
    onehot = (flat_routes[:, None] == jnp.arange(expert_count, dtype=jnp.int32)[None, :]).astype(
        jnp.int32
    )
    slot_rank = jnp.sum((jnp.cumsum(onehot, axis=0) - 1) * onehot, axis=1)
    slot_index = flat_routes * slot_cap + slot_rank
    source = (
        jnp.full((slot_total,), route_total, jnp.int32)
        .at[slot_index]
        .set(jnp.arange(route_total, dtype=jnp.int32))
    )
    table = jnp.concatenate(
        [
            jnp.concatenate(
                [
                    tokens,
                    (gates[:, k : k + 1] * grad_out.astype(jnp.float32)).astype(jnp.bfloat16),
                ],
                axis=1,
            )
            for k in range(route_count)
        ]
        + [jnp.zeros((1, 2 * model_width), jnp.bfloat16)],
        axis=0,
    )
    by_choice = jnp.where(
        source < route_total,
        (source % route_count) * tok_count + source // route_count,
        route_total,
    )
    both_recv = lax.all_to_all(table[by_choice], "exp", split_axis=0, concat_axis=0, tiled=True)
    x_recv = both_recv[:, :model_width]
    g_recv = both_recv[:, model_width:]
    full_all = lax.all_gather(
        jnp.stack([w_gate[0], w_up[0], w_down[0]], axis=0), "rep", axis=1, tiled=True
    )
    full_gate, full_up, full_down = full_all[0], full_all[1], full_all[2]
    pre_gate = jnp.dot(x_recv, full_gate, preferred_element_type=jnp.float32)
    pre_up = jnp.dot(x_recv, full_up, preferred_element_type=jnp.float32)
    hid_grad = jnp.dot(g_recv, full_down, preferred_element_type=jnp.float32)
    sig_gate = jax.nn.sigmoid(pre_gate)
    silu_gate = pre_gate * sig_gate
    hidden = (silu_gate * pre_up).astype(jnp.bfloat16)
    d_gate = (hid_grad * pre_up * sig_gate * (1.0 + pre_gate * (1.0 - sig_gate))).astype(
        jnp.bfloat16
    )
    d_up = (hid_grad * silu_gate).astype(jnp.bfloat16)
    row_grad = (against_cols(d_gate, full_gate) + against_cols(d_up, full_up)).astype(jnp.bfloat16)
    returned = lax.all_to_all(row_grad, "exp", split_axis=0, concat_axis=0, tiled=True)
    picked = returned[slot_index].reshape(tok_count, route_count, model_width)
    grad_in = jnp.sum(picked.astype(jnp.float32), axis=1).astype(jnp.bfloat16)
    stacked = lax.dot_general(
        jnp.stack([x_recv, x_recv, g_recv], axis=0),
        jnp.stack([d_gate, d_up, hidden], axis=0),
        (((1,), (1,)), ((0,), (0,))),
        preferred_element_type=jnp.float32,
    ).astype(jnp.bfloat16)
    summed = lax.psum_scatter(stacked, "rep", scatter_dimension=1, tiled=True)
    summed = summed.astype(jnp.float32)
    grad_gate = summed[0]
    grad_up = summed[1]
    grad_down = summed[2]
    return (grad_gate[None], grad_up[None], grad_down[None], grad_in)


def solution(mesh):
    placed = (
        P(("rep", "exp"), None),
        P(("rep", "exp"), None),
        P(("rep", "exp"), None),
        P(("rep", "exp"), None),
        P("exp", "rep", None),
        P("exp", "rep", None),
        P("exp", "rep", None),
    )
    return jax.shard_map(
        per_device,
        mesh=mesh,
        in_specs=placed,
        out_specs=(
            P("exp", "rep", None),
            P("exp", "rep", None),
            P("exp", "rep", None),
            P(("rep", "exp"), None),
        ),
        check_vma=False,
    )
```

```python
import jax
import jax.numpy as jnp
from jax import lax
from jax.sharding import PartitionSpec as P


def contract_rows(left, right):
    return lax.dot_general(
        left, right, (((0,), (0,)), ((), ())), preferred_element_type=jnp.float32
    )


def against_cols(left, right):
    return lax.dot_general(
        left, right, (((1,), (1,)), ((), ())), preferred_element_type=jnp.float32
    )


def per_device(tokens, grad_out, routes, gates, w_gate, w_up, w_down):
    tok_count, model_width = tokens.shape
    route_count = routes.shape[1]
    expert_count = lax.axis_size("exp")
    slot_cap = max(2, 2 * tok_count * route_count // expert_count)
    route_total = tok_count * route_count
    slot_total = expert_count * slot_cap
    flat_routes = routes.reshape(-1)
    onehot = (flat_routes[:, None] == jnp.arange(expert_count, dtype=jnp.int32)[None, :]).astype(
        jnp.int32
    )
    slot_rank = jnp.sum((jnp.cumsum(onehot, axis=0) - 1) * onehot, axis=1)
    slot_index = flat_routes * slot_cap + slot_rank
    source = (
        jnp.full((slot_total,), route_total, jnp.int32)
        .at[slot_index]
        .set(jnp.arange(route_total, dtype=jnp.int32))
    )
    table = jnp.concatenate(
        [
            jnp.concatenate(
                [
                    tokens,
                    (gates[:, k : k + 1] * grad_out.astype(jnp.float32)).astype(jnp.bfloat16),
                ],
                axis=1,
            )
            for k in range(route_count)
        ]
        + [jnp.zeros((1, 2 * model_width), jnp.bfloat16)],
        axis=0,
    )
    by_choice = jnp.where(
        source < route_total,
        (source % route_count) * tok_count + source // route_count,
        route_total,
    )
    both_recv = lax.all_to_all(table[by_choice], "exp", split_axis=0, concat_axis=0, tiled=True)
    x_recv = both_recv[:, :model_width]
    g_recv = both_recv[:, model_width:]
    full_all = lax.all_gather(
        jnp.stack([w_gate[0], w_up[0], w_down[0]], axis=0), "rep", axis=1, tiled=True
    )
    full_gate, full_up, full_down = full_all[0], full_all[1], full_all[2]
    pre_gate = jnp.dot(x_recv, full_gate, preferred_element_type=jnp.float32)
    pre_up = jnp.dot(x_recv, full_up, preferred_element_type=jnp.float32)
    hid_grad = jnp.dot(g_recv, full_down, preferred_element_type=jnp.float32)
    sig_gate = jax.nn.sigmoid(pre_gate)
    silu_gate = pre_gate * sig_gate
    hidden = (silu_gate * pre_up).astype(jnp.bfloat16)
    d_gate = (hid_grad * pre_up * sig_gate * (1.0 + pre_gate * (1.0 - sig_gate))).astype(
        jnp.bfloat16
    )
    d_up = (hid_grad * silu_gate).astype(jnp.bfloat16)
    row_grad = (against_cols(d_gate, full_gate) + against_cols(d_up, full_up)).astype(jnp.bfloat16)
    returned = lax.all_to_all(row_grad, "exp", split_axis=0, concat_axis=0, tiled=True)
    picked = returned[slot_index].reshape(tok_count, route_count, model_width)
    grad_in = jnp.sum(picked.astype(jnp.float32), axis=1).astype(jnp.bfloat16)
    stacked = jnp.zeros((3, model_width, d_gate.shape[1]), jnp.bfloat16)
    for which, part in enumerate(
        (
            contract_rows(x_recv, d_gate),
            contract_rows(x_recv, d_up),
            contract_rows(g_recv, hidden),
        )
    ):
        stacked = lax.dynamic_update_slice(stacked, part.astype(jnp.bfloat16)[None], (which, 0, 0))
    summed = lax.psum_scatter(stacked, "rep", scatter_dimension=1, tiled=True)
    summed = summed.astype(jnp.float32)
    grad_gate = summed[0]
    grad_up = summed[1]
    grad_down = summed[2]
    return (grad_gate[None], grad_up[None], grad_down[None], grad_in)


def solution(mesh):
    placed = (
        P(("rep", "exp"), None),
        P(("rep", "exp"), None),
        P(("rep", "exp"), None),
        P(("rep", "exp"), None),
        P("exp", "rep", None),
        P("exp", "rep", None),
        P("exp", "rep", None),
    )
    return jax.shard_map(
        per_device,
        mesh=mesh,
        in_specs=placed,
        out_specs=(
            P("exp", "rep", None),
            P("exp", "rep", None),
            P("exp", "rep", None),
            P(("rep", "exp"), None),
        ),
        check_vma=False,
    )
```

```python
import jax
import jax.numpy as jnp
from jax import lax
from jax.sharding import PartitionSpec as P


def contract_rows(left, right):
    return lax.dot_general(
        left, right, (((0,), (0,)), ((), ())), preferred_element_type=jnp.float32
    )


def against_cols(left, right):
    return lax.dot_general(
        left, right, (((1,), (1,)), ((), ())), preferred_element_type=jnp.float32
    )


def per_device(tokens, grad_out, routes, gates, w_gate, w_up, w_down):
    tok_count, model_width = tokens.shape
    route_count = routes.shape[1]
    expert_count = lax.axis_size("exp")
    slot_cap = max(2, 2 * tok_count * route_count // expert_count)
    route_total = tok_count * route_count
    slot_total = expert_count * slot_cap
    flat_routes = routes.reshape(-1)
    onehot = (flat_routes[:, None] == jnp.arange(expert_count, dtype=jnp.int32)[None, :]).astype(
        jnp.int32
    )
    slot_rank = jnp.sum((jnp.cumsum(onehot, axis=0) - 1) * onehot, axis=1)
    slot_index = flat_routes * slot_cap + slot_rank
    match = slot_index[None, :] == jnp.arange(slot_total, dtype=jnp.int32)[:, None]
    source = jnp.sum(
        jnp.where(match, jnp.arange(route_total, dtype=jnp.int32)[None, :], 0), axis=1
    ) + jnp.where(jnp.any(match, axis=1), 0, route_total)
    table = jnp.concatenate(
        [
            jnp.concatenate(
                [
                    tokens,
                    (gates[:, k : k + 1] * grad_out.astype(jnp.float32)).astype(jnp.bfloat16),
                ],
                axis=1,
            )
            for k in range(route_count)
        ]
        + [jnp.zeros((1, 2 * model_width), jnp.bfloat16)],
        axis=0,
    )
    by_choice = jnp.where(
        source < route_total,
        (source % route_count) * tok_count + source // route_count,
        route_total,
    )
    both_recv = lax.all_to_all(table[by_choice], "exp", split_axis=0, concat_axis=0, tiled=True)
    x_recv = both_recv[:, :model_width]
    g_recv = both_recv[:, model_width:]
    gate_up = lax.all_gather(jnp.stack([w_gate[0], w_up[0]], axis=0), "rep", axis=1, tiled=True)
    full_gate, full_up = gate_up[0], gate_up[1]
    full_down = lax.all_gather(w_down[0], "rep", axis=0, tiled=True)
    pre_gate = jnp.dot(x_recv, full_gate, preferred_element_type=jnp.float32)
    pre_up = jnp.dot(x_recv, full_up, preferred_element_type=jnp.float32)
    hid_grad = jnp.dot(g_recv, full_down, preferred_element_type=jnp.float32)
    sig_gate = jax.nn.sigmoid(pre_gate)
    silu_gate = pre_gate * sig_gate
    hidden = (silu_gate * pre_up).astype(jnp.bfloat16)
    d_gate = (hid_grad * pre_up * sig_gate * (1.0 + pre_gate * (1.0 - sig_gate))).astype(
        jnp.bfloat16
    )
    d_up = (hid_grad * silu_gate).astype(jnp.bfloat16)
    row_grad = (against_cols(d_gate, full_gate) + against_cols(d_up, full_up)).astype(jnp.bfloat16)
    returned = lax.all_to_all(row_grad, "exp", split_axis=0, concat_axis=0, tiled=True)
    picked = returned[slot_index].reshape(tok_count, route_count, model_width)
    grad_in = jnp.sum(picked.astype(jnp.float32), axis=1).astype(jnp.bfloat16)
    summed = lax.psum_scatter(
        jnp.stack(
            [
                contract_rows(x_recv, d_gate),
                contract_rows(x_recv, d_up),
                contract_rows(g_recv, hidden),
            ],
            axis=0,
        ).astype(jnp.bfloat16),
        "rep",
        scatter_dimension=1,
        tiled=True,
    )
    summed = summed.astype(jnp.float32)
    grad_gate = summed[0]
    grad_up = summed[1]
    grad_down = summed[2]
    return (grad_gate[None], grad_up[None], grad_down[None], grad_in)


def solution(mesh):
    placed = (
        P(("rep", "exp"), None),
        P(("rep", "exp"), None),
        P(("rep", "exp"), None),
        P(("rep", "exp"), None),
        P("exp", "rep", None),
        P("exp", "rep", None),
        P("exp", "rep", None),
    )
    return jax.shard_map(
        per_device,
        mesh=mesh,
        in_specs=placed,
        out_specs=(
            P("exp", "rep", None),
            P("exp", "rep", None),
            P("exp", "rep", None),
            P(("rep", "exp"), None),
        ),
        check_vma=False,
    )
```

```python
import jax
import jax.numpy as jnp
from jax import lax
from jax.sharding import PartitionSpec as P


def contract_rows(left, right):
    return lax.dot_general(
        left, right, (((0,), (0,)), ((), ())), preferred_element_type=jnp.float32
    )


def against_cols(left, right):
    return lax.dot_general(
        left, right, (((1,), (1,)), ((), ())), preferred_element_type=jnp.float32
    )


def per_device(tokens, grad_out, routes, gates, w_gate, w_up, w_down):
    tok_count, model_width = tokens.shape
    route_count = routes.shape[1]
    expert_count = lax.axis_size("exp")
    slot_cap = max(2, 2 * tok_count * route_count // expert_count)
    route_total = tok_count * route_count
    slot_total = expert_count * slot_cap
    flat_routes = routes.reshape(-1)
    onehot = (flat_routes[:, None] == jnp.arange(expert_count, dtype=jnp.int32)[None, :]).astype(
        jnp.int32
    )
    slot_rank = jnp.sum((jnp.cumsum(onehot, axis=0) - 1) * onehot, axis=1)
    slot_index = flat_routes * slot_cap + slot_rank
    source = (
        jnp.full((slot_total,), route_total, jnp.int32)
        .at[slot_index]
        .set(jnp.arange(route_total, dtype=jnp.int32))
    )
    table = jnp.concatenate(
        [
            jnp.concatenate(
                [
                    tokens,
                    (gates[:, k : k + 1] * grad_out.astype(jnp.float32)).astype(jnp.bfloat16),
                ],
                axis=1,
            )
            for k in range(route_count)
        ]
        + [jnp.zeros((1, 2 * model_width), jnp.bfloat16)],
        axis=0,
    )
    by_choice = jnp.where(
        source < route_total,
        (source % route_count) * tok_count + source // route_count,
        route_total,
    )
    both_recv = lax.all_to_all(table[by_choice], "exp", split_axis=0, concat_axis=0, tiled=True)
    x_recv = both_recv[:, :model_width]
    g_recv = both_recv[:, model_width:]
    full_all = lax.all_gather(
        jnp.stack([w_gate[0], w_up[0], w_down[0]], axis=0), "rep", axis=1, tiled=True
    )
    full_gate, full_up, full_down = full_all[0], full_all[1], full_all[2]
    ff = full_gate.shape[1]
    pre_both = jnp.dot(
        x_recv, jnp.concatenate([full_gate, full_up], axis=1), preferred_element_type=jnp.float32
    )
    pre_gate = pre_both[:, :ff]
    pre_up = pre_both[:, ff:]
    hid_grad = jnp.dot(g_recv, full_down, preferred_element_type=jnp.float32)
    sig_gate = jax.nn.sigmoid(pre_gate)
    silu_gate = pre_gate * sig_gate
    hidden = (silu_gate * pre_up).astype(jnp.bfloat16)
    d_gate = (hid_grad * pre_up * sig_gate * (1.0 + pre_gate * (1.0 - sig_gate))).astype(
        jnp.bfloat16
    )
    d_up = (hid_grad * silu_gate).astype(jnp.bfloat16)
    row_grad = (against_cols(d_gate, full_gate) + against_cols(d_up, full_up)).astype(jnp.bfloat16)
    returned = lax.all_to_all(row_grad, "exp", split_axis=0, concat_axis=0, tiled=True)
    picked = returned[slot_index].reshape(tok_count, route_count, model_width)
    grad_in = jnp.sum(picked.astype(jnp.float32), axis=1).astype(jnp.bfloat16)
    summed = lax.psum_scatter(
        jnp.stack(
            [
                contract_rows(x_recv, d_gate),
                contract_rows(x_recv, d_up),
                contract_rows(g_recv, hidden),
            ],
            axis=0,
        ).astype(jnp.bfloat16),
        "rep",
        scatter_dimension=1,
        tiled=True,
    )
    summed = summed.astype(jnp.float32)
    grad_gate = summed[0]
    grad_up = summed[1]
    grad_down = summed[2]
    return (grad_gate[None], grad_up[None], grad_down[None], grad_in)


def solution(mesh):
    placed = (
        P(("rep", "exp"), None),
        P(("rep", "exp"), None),
        P(("rep", "exp"), None),
        P(("rep", "exp"), None),
        P("exp", "rep", None),
        P("exp", "rep", None),
        P("exp", "rep", None),
    )
    return jax.shard_map(
        per_device,
        mesh=mesh,
        in_specs=placed,
        out_specs=(
            P("exp", "rep", None),
            P("exp", "rep", None),
            P("exp", "rep", None),
            P(("rep", "exp"), None),
        ),
        check_vma=False,
    )
```

```python
import jax
import jax.numpy as jnp
from jax import lax
from jax.sharding import PartitionSpec as P


def contract_rows(left, right):
    return lax.dot_general(
        left, right, (((0,), (0,)), ((), ())), preferred_element_type=jnp.float32
    )


def against_cols(left, right):
    return lax.dot_general(
        left, right, (((1,), (1,)), ((), ())), preferred_element_type=jnp.float32
    )


def per_device(tokens, grad_out, routes, gates, w_gate, w_up, w_down):
    tok_count, model_width = tokens.shape
    route_count = routes.shape[1]
    expert_count = lax.axis_size("exp")
    slot_cap = max(2, 2 * tok_count * route_count // expert_count)
    route_total = tok_count * route_count
    slot_total = expert_count * slot_cap
    flat_routes = routes.reshape(-1)
    onehot = (flat_routes[:, None] == jnp.arange(expert_count, dtype=jnp.int32)[None, :]).astype(
        jnp.int32
    )
    slot_rank = jnp.sum((jnp.cumsum(onehot, axis=0) - 1) * onehot, axis=1)
    slot_index = flat_routes * slot_cap + slot_rank
    match = slot_index[None, :] == jnp.arange(slot_total, dtype=jnp.int32)[:, None]
    source = jnp.sum(
        jnp.where(match, jnp.arange(route_total, dtype=jnp.int32)[None, :], 0), axis=1
    ) + jnp.where(jnp.any(match, axis=1), 0, route_total)
    table = jnp.concatenate(
        [
            jnp.concatenate(
                [
                    tokens,
                    (gates[:, k : k + 1] * grad_out.astype(jnp.float32)).astype(jnp.bfloat16),
                ],
                axis=1,
            )
            for k in range(route_count)
        ]
        + [jnp.zeros((1, 2 * model_width), jnp.bfloat16)],
        axis=0,
    )
    by_choice = jnp.where(
        source < route_total,
        (source % route_count) * tok_count + source // route_count,
        route_total,
    )
    both_recv = lax.all_to_all(table[by_choice], "exp", split_axis=0, concat_axis=0, tiled=True)
    x_recv = both_recv[:, :model_width]
    g_recv = both_recv[:, model_width:]
    full_all = lax.all_gather(
        jnp.stack([w_gate[0], w_up[0], w_down[0]], axis=0), "rep", axis=1, tiled=True
    )
    full_gate, full_up, full_down = full_all[0], full_all[1], full_all[2]
    pre_gate = jnp.dot(x_recv, full_gate, preferred_element_type=jnp.float32)
    pre_up = jnp.dot(x_recv, full_up, preferred_element_type=jnp.float32)
    hid_grad = jnp.dot(g_recv, full_down, preferred_element_type=jnp.float32)
    sig_gate = jax.nn.sigmoid(pre_gate)
    silu_gate = pre_gate * sig_gate
    hidden = (silu_gate * pre_up).astype(jnp.bfloat16)
    d_gate = (hid_grad * pre_up * sig_gate * (1.0 + pre_gate * (1.0 - sig_gate))).astype(
        jnp.bfloat16
    )
    d_up = (hid_grad * silu_gate).astype(jnp.bfloat16)
    row_grad = (against_cols(d_gate, full_gate) + against_cols(d_up, full_up)).astype(jnp.bfloat16)
    returned = lax.all_to_all(row_grad, "exp", split_axis=0, concat_axis=0, tiled=True)
    picked = returned[slot_index].reshape(tok_count, route_count, model_width)
    grad_in = jnp.sum(picked.astype(jnp.float32), axis=1).astype(jnp.bfloat16)
    summed = lax.psum_scatter(
        jnp.stack(
            [
                contract_rows(x_recv, d_gate),
                contract_rows(x_recv, d_up),
                contract_rows(g_recv, hidden),
            ],
            axis=0,
        ).astype(jnp.bfloat16),
        "rep",
        scatter_dimension=1,
        tiled=True,
    )
    summed = summed.astype(jnp.float32)
    grad_gate = summed[0]
    grad_up = summed[1]
    grad_down = summed[2]
    return (grad_gate[None], grad_up[None], grad_down[None], grad_in)


def solution(mesh):
    placed = (
        P(("rep", "exp"), None),
        P(("rep", "exp"), None),
        P(("rep", "exp"), None),
        P(("rep", "exp"), None),
        P("exp", "rep", None),
        P("exp", "rep", None),
        P("exp", "rep", None),
    )
    return jax.shard_map(
        per_device,
        mesh=mesh,
        in_specs=placed,
        out_specs=(
            P("exp", "rep", None),
            P("exp", "rep", None),
            P("exp", "rep", None),
            P(("rep", "exp"), None),
        ),
        check_vma=False,
    )
```

```python
import jax
import jax.numpy as jnp
from jax import lax
from jax.sharding import PartitionSpec as P


def contract_rows(left, right):
    return lax.dot_general(
        left, right, (((0,), (0,)), ((), ())), preferred_element_type=jnp.float32
    )


def against_cols(left, right):
    return lax.dot_general(
        left, right, (((1,), (1,)), ((), ())), preferred_element_type=jnp.float32
    )


def per_device(tokens, grad_out, routes, gates, w_gate, w_up, w_down):
    tok_count, model_width = tokens.shape
    route_count = routes.shape[1]
    expert_count = lax.axis_size("exp")
    slot_cap = max(2, 2 * tok_count * route_count // expert_count)
    route_total = tok_count * route_count
    slot_total = expert_count * slot_cap
    flat_routes = routes.reshape(-1)
    onehot = (flat_routes[:, None] == jnp.arange(expert_count, dtype=jnp.int32)[None, :]).astype(
        jnp.int32
    )
    slot_rank = jnp.sum((jnp.cumsum(onehot, axis=0) - 1) * onehot, axis=1)
    slot_index = flat_routes * slot_cap + slot_rank
    match = slot_index[None, :] == jnp.arange(slot_total, dtype=jnp.int32)[:, None]
    source = jnp.sum(
        jnp.where(match, jnp.arange(route_total, dtype=jnp.int32)[None, :], 0), axis=1
    ) + jnp.where(jnp.any(match, axis=1), 0, route_total)
    table = jnp.concatenate(
        [
            jnp.concatenate(
                [
                    tokens,
                    (gates[:, k : k + 1] * grad_out.astype(jnp.float32)).astype(jnp.bfloat16),
                ],
                axis=1,
            )
            for k in range(route_count)
        ]
        + [jnp.zeros((1, 2 * model_width), jnp.bfloat16)],
        axis=0,
    )
    by_choice = jnp.where(
        source < route_total,
        (source % route_count) * tok_count + source // route_count,
        route_total,
    )
    both_recv = lax.all_to_all(table[by_choice], "exp", split_axis=0, concat_axis=0, tiled=True)
    x_recv = both_recv[:, :model_width]
    g_recv = both_recv[:, model_width:]
    full_all = lax.all_gather(
        jnp.stack([w_gate[0], w_up[0], w_down[0]], axis=0), "rep", axis=1, tiled=True
    )
    full_gate, full_up, full_down = full_all[0], full_all[1], full_all[2]
    pre_both = lax.dot_general(
        x_recv, full_all[0:2], (((1,), (1,)), ((), ())), preferred_element_type=jnp.float32
    )
    pre_gate = pre_both[:, 0, :]
    pre_up = pre_both[:, 1, :]
    hid_grad = jnp.dot(g_recv, full_down, preferred_element_type=jnp.float32)
    sig_gate = jax.nn.sigmoid(pre_gate)
    silu_gate = pre_gate * sig_gate
    hidden = (silu_gate * pre_up).astype(jnp.bfloat16)
    d_gate = (hid_grad * pre_up * sig_gate * (1.0 + pre_gate * (1.0 - sig_gate))).astype(
        jnp.bfloat16
    )
    d_up = (hid_grad * silu_gate).astype(jnp.bfloat16)
    row_grad = (against_cols(d_gate, full_gate) + against_cols(d_up, full_up)).astype(jnp.bfloat16)
    returned = lax.all_to_all(row_grad, "exp", split_axis=0, concat_axis=0, tiled=True)
    picked = returned[slot_index].reshape(tok_count, route_count, model_width)
    grad_in = jnp.sum(picked.astype(jnp.float32), axis=1).astype(jnp.bfloat16)
    summed = lax.psum_scatter(
        jnp.stack(
            [
                contract_rows(x_recv, d_gate),
                contract_rows(x_recv, d_up),
                contract_rows(g_recv, hidden),
            ],
            axis=0,
        ).astype(jnp.bfloat16),
        "rep",
        scatter_dimension=1,
        tiled=True,
    )
    summed = summed.astype(jnp.float32)
    grad_gate = summed[0]
    grad_up = summed[1]
    grad_down = summed[2]
    return (grad_gate[None], grad_up[None], grad_down[None], grad_in)


def solution(mesh):
    placed = (
        P(("rep", "exp"), None),
        P(("rep", "exp"), None),
        P(("rep", "exp"), None),
        P(("rep", "exp"), None),
        P("exp", "rep", None),
        P("exp", "rep", None),
        P("exp", "rep", None),
    )
    return jax.shard_map(
        per_device,
        mesh=mesh,
        in_specs=placed,
        out_specs=(
            P("exp", "rep", None),
            P("exp", "rep", None),
            P("exp", "rep", None),
            P(("rep", "exp"), None),
        ),
        check_vma=False,
    )
```
